256 devices in a mesh: ctx: 64 (over z, x_hi, y), hd: 4 (over x_lo, core).
Axes of the slice: x: 4 (x_hi: 2, x_lo: 2; x = x_hi * 2 + x_lo), y: 4, z: 8, core: 2. Of those that a mesh axis runs over, the one named last changes fastest.
Arguments:
- tokens: bfloat16 [32768, 4096], P('ctx'), may hold values from -6 to 6
- w_query: bfloat16 [4096, 2048], P('ctx', 'hd'), may hold values from -0.09375 to 0.09375
- w_key: bfloat16 [4096, 2048], P('ctx', 'hd'), may hold values from -0.09375 to 0.09375
- w_value: bfloat16 [4096, 2048], P('ctx', 'hd'), may hold values from -0.09375 to 0.09375
Outputs:
- attended: bfloat16 [32768, 2048], P('ctx', 'hd')
The draws below stay inside these ranges and needn't reach their ends.
All inputs are finite; a program needn't handle non-finite values.
Results may differ from the reference program's by a relative error of at most 0.0065.
Values may be sent and summed in bfloat16 or wider, within the bound.
No kernel may reach another device: no remote copies, remote signals or barrier semaphores. Data moves between devices by JAX's collectives and lax.ppermute only.
A program may use at most 64 MiB of HBM per device.

```python
import jax
import jax.numpy as jnp
from jax import lax

D = 4096
H = 16
DH = 128
BLOCK = 512
TOKENS = 32768


def block_scale(rng, extent, split, least, high):
    level, own = 1.0, jax.random.fold_in(rng, 6)
    for axis_at, shards_of in split:
        draws = jnp.exp(jax.random.uniform(jax.random.fold_in(own, axis_at), (shards_of,), jnp.float32, least / len(split), high / len(split)))
        level = level * jnp.repeat(draws, extent[axis_at] // shards_of).reshape([-1 if axis == axis_at else 1 for axis in range(len(extent))])
    return level


def scatter_about(stream_key, dims, deviation, bound, cuts=(), kind=jnp.bfloat16):
    entries = deviation * jax.random.normal(stream_key, dims, jnp.float32)
    if cuts:
        entries = entries * block_scale(stream_key, dims, cuts, -0.22, 0.18)
    return jnp.clip(entries, -bound, bound).astype(kind)


def setup_inputs(seed: int = 0) -> dict:
    keys = jax.random.split(jax.random.key(seed), 5)
    tokens = scatter_about(keys[0], (TOKENS, D), 1.0, 6.0, ((0, 64),))
    w_query = scatter_about(keys[1], (D, H * DH), D ** -0.5, 0.09375, ((0, 64), (1, 4)))
    w_key = scatter_about(keys[2], (D, H * DH), D ** -0.5, 0.09375, ((0, 64), (1, 4)))
    w_value = scatter_about(keys[3], (D, H * DH), D ** -0.5, 0.09375, ((0, 64), (1, 4)))
    return dict(tokens=tokens, w_query=w_query, w_key=w_key, w_value=w_value)


epsilon = 1e-06

def reference(tokens, w_query, w_key, w_value):
    query_all = jnp.dot(tokens, w_query, preferred_element_type=jnp.float32).astype(jnp.bfloat16)
    key_all = jnp.dot(tokens, w_key, preferred_element_type=jnp.float32).astype(jnp.bfloat16)
    value_all = jnp.dot(tokens, w_value, preferred_element_type=jnp.float32).astype(jnp.bfloat16)
    block_count = TOKENS // BLOCK
    query_blocks = query_all.reshape(block_count, BLOCK, H, DH)
    key_blocks = key_all.reshape(block_count, BLOCK, H, DH)
    value_blocks = value_all.reshape(block_count, BLOCK, H, DH)
    causal_mask = jnp.tril(jnp.ones((BLOCK, BLOCK), dtype=bool))

    def one_block(kv_state, inputs):
        query_rows, key_rows, value_rows = inputs
        query_wide = query_rows.astype(jnp.float32)
        key_wide = key_rows.astype(jnp.float32)
        value_wide = value_rows.astype(jnp.float32)
        scores = jnp.einsum('qhd,khd->hqk', query_wide, key_wide)
        scores = jnp.where(causal_mask[None], scores, 0.0).astype(jnp.bfloat16)
        local_term = jnp.einsum('hqk,khd->qhd', scores.astype(jnp.float32), value_wide)
        carried = jnp.einsum('qhd,hde->qhe', query_wide, kv_state, precision=lax.Precision.HIGHEST)
        attended_raw = carried + local_term
        scale_inv = lax.rsqrt(lax.optimization_barrier(jnp.mean(attended_raw * attended_raw, axis=-1, keepdims=True)) + epsilon)
        attended = (attended_raw * scale_inv).astype(jnp.bfloat16)
        new_state = kv_state + jnp.einsum('khd,khe->hde', key_wide, value_wide)
        return (new_state, attended)
    start_state = jnp.zeros((H, DH, DH), jnp.float32)
    final_state, attended = lax.scan(one_block, start_state, (query_blocks, key_blocks, value_blocks))
    return attended.reshape(TOKENS, H * DH)
```

```python
import jax
import jax.numpy as jnp
from jax import lax
from jax.sharding import Mesh
from jax.sharding import PartitionSpec as P

DH = 128
BLOCK = 512
epsilon = 1e-06

FINE = (("z", 8), ("xh", 2), ("y", 4))
CTX = tuple(name for name, _ in FINE)
W_ORDER = ("xh", "y", "z")
KV_MODE = "hier"


def fine_mesh(mesh):
    sizes = [n for _, n in FINE]
    devices = mesh.devices.reshape(*sizes, mesh.devices.shape[1])
    return Mesh(devices, (*CTX, "hd"))


def gather_weights(w3):
    g = w3
    for name in W_ORDER:
        g = lax.all_gather(g, name, axis=1, tiled=False)
    got = list(reversed(W_ORDER))
    perm = [0] + [1 + got.index(name) for name in CTX] + [4, 5]
    return g, got


def prefix_over_ctx(state):
    def exclusive(g, name):
        idx = lax.axis_index(name)
        n = g.shape[0]
        mask = (jnp.arange(n) < idx).reshape(n, *([1] * (g.ndim - 1)))
        return jnp.sum(jnp.where(mask, g, 0.0), axis=0), jnp.sum(g, axis=0)

    if KV_MODE == "hier":
        total = state
        out = jnp.zeros_like(state)
        for name in reversed(CTX):
            g = lax.all_gather(total, name)
            before, total = exclusive(g, name)
            out = out + before
        return out
    else:
        g = lax.all_gather(state, CTX)
        return exclusive(g, CTX)[0]


def local(tokens, w_query, w_key, w_value):
    tok_rows, width = tokens.shape
    width_group = w_query.shape[1]
    head_count = width_group // DH
    w3 = jnp.stack([w_query, w_key, w_value])
    g, got = gather_weights(w3)
    sizes = dict(FINE)
    tok = tokens.reshape(tok_rows, *[sizes[n] for n in CTX], w3.shape[1])
    t_labels = "t" + "".join({"z": "a", "xh": "b", "y": "c"}[n] for n in CTX) + "k"
    g_labels = "w" + "".join({"z": "a", "xh": "b", "y": "c"}[n] for n in got) + "kn"
    qkv = jnp.einsum(f"{t_labels},{g_labels}->wtn", tok, g, preferred_element_type=jnp.float32)
    qkv = qkv.astype(jnp.bfloat16).reshape(3, tok_rows, head_count, DH)
    query_rows, key_rows, value_rows = qkv[0], qkv[1], qkv[2]
    causal_mask = jnp.tril(jnp.ones((BLOCK, BLOCK), dtype=bool))
    scores = jnp.einsum("qhd,khd->hqk", query_rows, key_rows, preferred_element_type=jnp.float32)
    scores = jnp.where(causal_mask[None], scores, 0.0).astype(jnp.bfloat16)
    local_term = jnp.einsum("hqk,khd->qhd", scores, value_rows, preferred_element_type=jnp.float32)
    own_total = jnp.einsum("khd,khe->hde", key_rows, value_rows, preferred_element_type=jnp.float32)
    start_state = prefix_over_ctx(own_total)
    carried = jnp.einsum(
        "qhd,hde->qhe",
        query_rows.astype(jnp.float32),
        start_state,
        precision=lax.Precision.HIGHEST,
    )
    attended_raw = carried + local_term
    scale_inv = lax.rsqrt(jnp.mean(attended_raw * attended_raw, axis=-1, keepdims=True) + epsilon)
    return (attended_raw * scale_inv).astype(jnp.bfloat16).reshape(tok_rows, width_group)


def solution(mesh):
    fine = fine_mesh(mesh)
    return jax.shard_map(
        local,
        mesh=fine,
        in_specs=(P(CTX, None), P(CTX, "hd"), P(CTX, "hd"), P(CTX, "hd")),
        out_specs=P(CTX, "hd"),
        check_vma=False,
    )
```

```python
import jax
import jax.numpy as jnp
from jax import lax
from jax.sharding import Mesh
from jax.sharding import PartitionSpec as P

DH = 128
BLOCK = 512
epsilon = 1e-06

FINE = (("z", 8), ("xh", 2), ("y", 4))
CTX = tuple(name for name, _ in FINE)
SIZES = dict(FINE)


def fine_mesh(mesh):
    devices = mesh.devices.reshape(*SIZES.values(), mesh.devices.shape[1])
    return Mesh(devices, (*CTX, "hd"))


def ring_values(x, name, n):
    right = [(j, (j + 1) % n) for j in range(n)]
    left = [(j, (j - 1) % n) for j in range(n)]
    got = []
    r = l = x
    for k in range(1, n // 2 + 1):
        r = lax.ppermute(r, name, right)
        got.append((k, r))
        if k < n - k:
            l = lax.ppermute(l, name, left)
            got.append((n - k, l))
    return got


def ring_gather(x, name, axis):
    n = SIZES[name]
    by_ahead = {0: x}
    for k, v in ring_values(x, name, n):
        by_ahead[(n - k) % n] = v
    stacked = jnp.stack([by_ahead[m] for m in range(n)], axis=axis)
    return jnp.roll(stacked, lax.axis_index(name), axis=axis)


def exclusive_and_total(x, name):
    n = SIZES[name]
    idx = lax.axis_index(name)
    before = jnp.zeros_like(x)
    total = x
    for k, v in ring_values(x, name, n):
        before = before + jnp.where(k <= idx, v, 0.0)
        total = total + v
    return before, total


def exclusive_scan(x, name):
    n = SIZES[name]
    e = lax.ppermute(x, name, [(j, j + 1) for j in range(n - 1)])
    d = 1
    while d < n:
        e = e + lax.ppermute(e, name, [(j, j + d) for j in range(n - d)])
        d *= 2
    return e


def prefix_over_ctx(state):
    before_y, total_y = exclusive_and_total(state, "y")
    before_x, total_xy = exclusive_and_total(total_y, "xh")
    return exclusive_scan(total_xy, "z") + before_x + before_y


def project(tokens, ws, split):
    w = jnp.stack(ws)
    g = lax.all_gather(w, "xh", axis=1)
    a, b = g[..., :split], g[..., split:]
    a = ring_gather(a, "y", axis=1)
    b = lax.all_gather(b, "z", axis=1)
    a = lax.all_gather(a, "z", axis=1)
    b = ring_gather(b, "y", axis=1)
    t = tokens.shape[0]
    k = w.shape[1]
    tok = tokens.reshape(t, SIZES["z"], SIZES["xh"], SIZES["y"], k)
    tok_a = tok.transpose(0, 1, 3, 2, 4).reshape(t, -1)
    tok_b = tok.transpose(0, 3, 1, 2, 4).reshape(t, -1)
    out_a = jnp.einsum("tk,wkn->wtn", tok_a, a.reshape(len(ws), -1, split), preferred_element_type=jnp.float32)
    out_b = jnp.einsum("tk,wkn->wtn", tok_b, b.reshape(len(ws), -1, w.shape[2] - split), preferred_element_type=jnp.float32)
    return jnp.concatenate([out_a, out_b], axis=-1)


def local(tokens, w_query, w_key, w_value):
    tok_rows = tokens.shape[0]
    width_group = w_query.shape[1]
    head_count = width_group // DH
    split = width_group // 2
    kv = project(tokens, [w_key, w_value], split).astype(jnp.bfloat16).reshape(2, tok_rows, head_count, DH)
    key_rows, value_rows = kv[0], kv[1]
    own_total = jnp.einsum("khd,khe->hde", key_rows, value_rows, preferred_element_type=jnp.float32)
    start_state = prefix_over_ctx(own_total)
    query_rows = project(tokens, [w_query], split).astype(jnp.bfloat16).reshape(tok_rows, head_count, DH)
    causal_mask = jnp.tril(jnp.ones((BLOCK, BLOCK), dtype=bool))
    scores = jnp.einsum("qhd,khd->hqk", query_rows, key_rows, preferred_element_type=jnp.float32)
    scores = jnp.where(causal_mask[None], scores, 0.0).astype(jnp.bfloat16)
    local_term = jnp.einsum("hqk,khd->qhd", scores, value_rows, preferred_element_type=jnp.float32)
    carried = jnp.einsum(
        "qhd,hde->qhe",
        query_rows.astype(jnp.float32),
        start_state,
        precision=lax.Precision.HIGHEST,
    )
    attended_raw = carried + local_term
    scale_inv = lax.rsqrt(jnp.mean(attended_raw * attended_raw, axis=-1, keepdims=True) + epsilon)
    return (attended_raw * scale_inv).astype(jnp.bfloat16).reshape(tok_rows, width_group)


def solution(mesh):
    fine = fine_mesh(mesh)
    return jax.shard_map(
        local,
        mesh=fine,
        in_specs=(P(CTX, None), P(CTX, "hd"), P(CTX, "hd"), P(CTX, "hd")),
        out_specs=P(CTX, "hd"),
        check_vma=False,
    )
```

```python
import jax
import jax.numpy as jnp
from jax import lax
from jax.sharding import Mesh
from jax.sharding import PartitionSpec as P

DH = 128
BLOCK = 512
epsilon = 1e-06

FINE = (("z", 8), ("xh", 2), ("y", 4))
CTX = tuple(name for name, _ in FINE)
SIZES = dict(FINE)


def fine_mesh(mesh):
    devices = mesh.devices.reshape(*SIZES.values(), mesh.devices.shape[1])
    return Mesh(devices, (*CTX, "hd"))


def ring_values(x, name, n):
    right = [(j, (j + 1) % n) for j in range(n)]
    left = [(j, (j - 1) % n) for j in range(n)]
    got = []
    r = l = x
    for k in range(1, n // 2 + 1):
        r = lax.ppermute(r, name, right)
        got.append((k, r))
        if k < n - k:
            l = lax.ppermute(l, name, left)
            got.append((n - k, l))
    return got


def ring_gather(x, name, axis):
    n = SIZES[name]
    by_ahead = {0: x}
    for k, v in ring_values(x, name, n):
        by_ahead[(n - k) % n] = v
    stacked = jnp.stack([by_ahead[m] for m in range(n)], axis=axis)
    return jnp.roll(stacked, lax.axis_index(name), axis=axis)


def direct_values(x, name, n):
    size = SIZES[name]
    got = []
    for k in range(1, n):
        pairs = [(j, j - j % n + (j % n + k) % n) for j in range(size)]
        got.append((k, lax.ppermute(x, name, pairs)))
    return got


def exclusive_and_total(x, name, n=None):
    n = n or SIZES[name]
    idx = lax.axis_index(name) % n
    before = jnp.zeros_like(x)
    total = x
    for k, v in direct_values(x, name, n):
        before = before + jnp.where(k <= idx, v, 0.0)
        total = total + v
    return before, total


def prefix_over_ctx(state):
    before_y, total_y = exclusive_and_total(state, "y")
    before_x, total_xy = exclusive_and_total(total_y, "xh")
    half = SIZES["z"] // 2
    before_zl, total_zl = exclusive_and_total(total_xy, "z", half)
    other = lax.ppermute(total_zl, "z", [(j, (j + half) % SIZES["z"]) for j in range(SIZES["z"])])
    before_zh = jnp.where(lax.axis_index("z") >= half, other, 0.0)
    return before_zh + before_zl + before_x + before_y


def project(tokens, ws, split):
    w = jnp.stack(ws)
    g = lax.all_gather(w, "xh", axis=1)
    a, b = g[..., :split], g[..., split:]
    a = ring_gather(a, "y", axis=1)
    b = ring_gather(b, "z", axis=1)
    t = tokens.shape[0]
    k = w.shape[1]
    tok = tokens.reshape(t, SIZES["z"], SIZES["xh"], SIZES["y"], k)
    tok_a = jnp.roll(tok.transpose(1, 0, 3, 2, 4), -lax.axis_index("z"), axis=0).reshape(SIZES["z"], t, -1)
    tok_b = jnp.roll(tok.transpose(3, 0, 1, 2, 4), -lax.axis_index("y"), axis=0).reshape(SIZES["y"], t, -1)

    def last_stage(x, name, toks):
        n = SIZES[name]
        pieces = [(0, x)] + [((n - d) % n, v) for d, v in ring_values(x, name, n)]
        out = None
        for m, v in pieces:
            part = jnp.einsum(
                "tk,wkn->wtn", toks[m], v.reshape(len(ws), -1, v.shape[-1]), preferred_element_type=jnp.float32
            )
            out = part if out is None else out + part
        return out

    out_a = last_stage(a, "z", tok_a)
    out_b = last_stage(b, "y", tok_b)
    return jnp.concatenate([out_a, out_b], axis=-1)


def local(tokens, w_query, w_key, w_value):
    tok_rows = tokens.shape[0]
    width_group = w_query.shape[1]
    head_count = width_group // DH
    split = width_group // 2
    qkv = project(tokens, [w_query, w_key, w_value], split).astype(jnp.bfloat16)
    qkv = qkv.reshape(3, tok_rows, head_count, DH)
    query_rows, key_rows, value_rows = qkv[0], qkv[1], qkv[2]
    own_total = jnp.einsum("khd,khe->hde", key_rows, value_rows, preferred_element_type=jnp.float32)
    start_state = prefix_over_ctx(own_total)
    causal_mask = jnp.tril(jnp.ones((BLOCK, BLOCK), dtype=bool))
    scores = jnp.einsum("qhd,khd->hqk", query_rows, key_rows, preferred_element_type=jnp.float32)
    scores = jnp.where(causal_mask[None], scores, 0.0).astype(jnp.bfloat16)
    local_term = jnp.einsum("hqk,khd->qhd", scores, value_rows, preferred_element_type=jnp.float32)
    carried = jnp.einsum(
        "qhd,hde->qhe",
        query_rows.astype(jnp.float32),
        start_state,
        precision=lax.Precision.HIGHEST,
    )
    attended_raw = carried + local_term
    scale_inv = lax.rsqrt(jnp.mean(attended_raw * attended_raw, axis=-1, keepdims=True) + epsilon)
    return (attended_raw * scale_inv).astype(jnp.bfloat16).reshape(tok_rows, width_group)


def solution(mesh):
    fine = fine_mesh(mesh)
    return jax.shard_map(
        local,
        mesh=fine,
        in_specs=(P(CTX, None), P(CTX, "hd"), P(CTX, "hd"), P(CTX, "hd")),
        out_specs=P(CTX, "hd"),
        check_vma=False,
    )
```

```python
import jax
import jax.numpy as jnp
from jax import lax
from jax.sharding import Mesh
from jax.sharding import PartitionSpec as P

DH = 128
BLOCK = 512
epsilon = 1e-06

FINE = (("z", 8), ("xh", 2), ("y", 4))
CTX = tuple(name for name, _ in FINE)
SIZES = dict(FINE)


def fine_mesh(mesh):
    devices = mesh.devices.reshape(*SIZES.values(), mesh.devices.shape[1])
    return Mesh(devices, (*CTX, "hd"))


def ring_values(x, name, n):
    right = [(j, (j + 1) % n) for j in range(n)]
    left = [(j, (j - 1) % n) for j in range(n)]
    got = []
    r = l = x
    for k in range(1, n // 2 + 1):
        r = lax.ppermute(r, name, right)
        got.append((k, r))
        if k < n - k:
            l = lax.ppermute(l, name, left)
            got.append((n - k, l))
    return got


def ring_gather(x, name, axis):
    n = SIZES[name]
    by_ahead = {0: x}
    for k, v in ring_values(x, name, n):
        by_ahead[(n - k) % n] = v
    stacked = jnp.stack([by_ahead[m] for m in range(n)], axis=axis)
    return jnp.roll(stacked, lax.axis_index(name), axis=axis)


def direct_values(x, name, n):
    size = SIZES[name]
    got = []
    for k in range(1, n):
        pairs = [(j, j - j % n + (j % n + k) % n) for j in range(size)]
        got.append((k, lax.ppermute(x, name, pairs)))
    return got


def exclusive_and_total(x, name, n=None):
    n = n or SIZES[name]
    idx = lax.axis_index(name) % n
    before = jnp.zeros_like(x)
    total = x
    for k, v in direct_values(x, name, n):
        before = before + jnp.where(k <= idx, v, 0.0)
        total = total + v
    return before, total


def prefix_over_ctx(state):
    before_y, total_y = exclusive_and_total(state, "y")
    before_x, total_xy = exclusive_and_total(total_y, "xh")
    half = SIZES["z"] // 2
    before_zl, total_zl = exclusive_and_total(total_xy, "z", half)
    other = lax.ppermute(total_zl, "z", [(j, (j + half) % SIZES["z"]) for j in range(SIZES["z"])])
    before_zh = jnp.where(lax.axis_index("z") >= half, other, 0.0)
    return before_zh + before_zl + before_x + before_y


def project(tokens, ws, split):
    w = jnp.stack(ws)
    g = lax.all_gather(w, "xh", axis=1)
    a, b = g[..., :split], g[..., split:]
    a = ring_gather(a, "y", axis=1)
    b = ring_gather(b, "z", axis=1)
    t = tokens.shape[0]
    k = w.shape[1]
    tok = tokens.reshape(t, SIZES["z"], SIZES["xh"], SIZES["y"], k)
    tok_a = jnp.roll(tok.transpose(1, 0, 3, 2, 4), -lax.axis_index("z"), axis=0).reshape(SIZES["z"], t, -1)
    tok_b = jnp.roll(tok.transpose(3, 0, 1, 2, 4), -lax.axis_index("y"), axis=0).reshape(SIZES["y"], t, -1)

    def last_stage(x, name, toks):
        n = SIZES[name]
        count = len(ws)
        x = x.reshape(count, -1, k, x.shape[-1])
        toks = toks.reshape(n, t, -1, k)
        right = [(j, (j + 1) % n) for j in range(n)]
        left = [(j, (j - 1) % n) for j in range(n)]
        half = k // 2
        pieces = [(0, x, 0, k)]
        r = l = x
        for d in range(1, n // 2 + 1):
            if d < n - d:
                r = lax.ppermute(r, name, right)
                l = lax.ppermute(l, name, left)
                pieces += [(n - d, r, 0, k), (d, l, 0, k)]
            else:
                pieces.append((d, lax.ppermute(r[:, :, :half], name, right), 0, half))
                pieces.append((d, lax.ppermute(l[:, :, half:], name, left), half, k))
        out = None
        for m, v, lo, hi in pieces:
            part = jnp.einsum("tjk,wjkn->wtn", toks[m][:, :, lo:hi], v, preferred_element_type=jnp.float32)
            out = part if out is None else out + part
        return out

    out_a = last_stage(a, "z", tok_a)
    out_b = last_stage(b, "y", tok_b)
    return jnp.concatenate([out_a, out_b], axis=-1)


def local(tokens, w_query, w_key, w_value):
    tok_rows = tokens.shape[0]
    width_group = w_query.shape[1]
    head_count = width_group // DH
    split = width_group // 2
    qkv = project(tokens, [w_query, w_key, w_value], split).astype(jnp.bfloat16)
    qkv = qkv.reshape(3, tok_rows, head_count, DH)
    query_rows, key_rows, value_rows = qkv[0], qkv[1], qkv[2]
    own_total = jnp.einsum("khd,khe->hde", key_rows, value_rows, preferred_element_type=jnp.float32)
    start_state = prefix_over_ctx(own_total)
    causal_mask = jnp.tril(jnp.ones((BLOCK, BLOCK), dtype=bool))
    scores = jnp.einsum("qhd,khd->hqk", query_rows, key_rows, preferred_element_type=jnp.float32)
    scores = jnp.where(causal_mask[None], scores, 0.0).astype(jnp.bfloat16)
    local_term = jnp.einsum("hqk,khd->qhd", scores, value_rows, preferred_element_type=jnp.float32)
    carried = jnp.einsum(
        "qhd,hde->qhe",
        query_rows.astype(jnp.float32),
        start_state,
        precision=lax.Precision.HIGHEST,
    )
    attended_raw = carried + local_term
    scale_inv = lax.rsqrt(jnp.mean(attended_raw * attended_raw, axis=-1, keepdims=True) + epsilon)
    return (attended_raw * scale_inv).astype(jnp.bfloat16).reshape(tok_rows, width_group)


def solution(mesh):
    fine = fine_mesh(mesh)
    return jax.shard_map(
        local,
        mesh=fine,
        in_specs=(P(CTX, None), P(CTX, "hd"), P(CTX, "hd"), P(CTX, "hd")),
        out_specs=P(CTX, "hd"),
        check_vma=False,
    )
```

```python
import jax
import jax.numpy as jnp
from jax import lax
from jax.sharding import Mesh
from jax.sharding import PartitionSpec as P

DH = 128
BLOCK = 512
epsilon = 1e-06

FINE = (("z", 8), ("xh", 2), ("y", 4))
CTX = tuple(name for name, _ in FINE)
SIZES = dict(FINE)


def fine_mesh(mesh):
    devices = mesh.devices.reshape(*SIZES.values(), mesh.devices.shape[1])
    return Mesh(devices, (*CTX, "hd"))


def ring_values(x, name, n):
    right = [(j, (j + 1) % n) for j in range(n)]
    left = [(j, (j - 1) % n) for j in range(n)]
    got = []
    r = l = x
    for k in range(1, n // 2 + 1):
        r = lax.ppermute(r, name, right)
        got.append((k, r))
        if k < n - k:
            l = lax.ppermute(l, name, left)
            got.append((n - k, l))
    return got


def ring_gather(x, name, axis):
    n = SIZES[name]
    by_ahead = {0: x}
    for k, v in ring_values(x, name, n):
        by_ahead[(n - k) % n] = v
    stacked = jnp.stack([by_ahead[m] for m in range(n)], axis=axis)
    return jnp.roll(stacked, lax.axis_index(name), axis=axis)


def direct_values(x, name, n):
    size = SIZES[name]
    got = []
    for k in range(1, n):
        pairs = [(j, j - j % n + (j % n + k) % n) for j in range(size)]
        got.append((k, lax.ppermute(x, name, pairs)))
    return got


def exclusive_and_total(x, name, n=None):
    n = n or SIZES[name]
    idx = lax.axis_index(name) % n
    before = jnp.zeros_like(x)
    total = x
    for k, v in direct_values(x, name, n):
        before = before + jnp.where(k <= idx, v, 0.0)
        total = total + v
    return before, total


def prefix_over_ctx(state):
    before_y, total_y = exclusive_and_total(state, "y")
    before_x, total_xy = exclusive_and_total(total_y, "xh")
    half = SIZES["z"] // 2
    before_zl, total_zl = exclusive_and_total(total_xy, "z", half)
    other = lax.ppermute(total_zl, "z", [(j, (j + half) % SIZES["z"]) for j in range(SIZES["z"])])
    before_zh = jnp.where(lax.axis_index("z") >= half, other, 0.0)
    return before_zh + before_zl + before_x + before_y


def project(tokens, ws, split):
    w = jnp.stack(ws)
    other = lax.ppermute(w, "xh", [(0, 1), (1, 0)])
    g = jnp.roll(jnp.stack([w, other], axis=1), lax.axis_index("xh"), axis=1)
    a, b = g[..., :split], g[..., split:]
    a = ring_gather(a, "y", axis=1)
    b = ring_gather(b, "z", axis=1)
    t = tokens.shape[0]
    k = w.shape[1]
    tok = tokens.reshape(t, SIZES["z"], SIZES["xh"], SIZES["y"], k)
    tok_a = jnp.roll(tok.transpose(1, 0, 3, 2, 4), -lax.axis_index("z"), axis=0).reshape(SIZES["z"], t, -1)
    tok_b = jnp.roll(tok.transpose(3, 0, 1, 2, 4), -lax.axis_index("y"), axis=0).reshape(SIZES["y"], t, -1)

    def last_stage(x, name, toks):
        n = SIZES[name]
        count = len(ws)
        x = x.reshape(count, -1, k, x.shape[-1])
        toks = toks.reshape(n, t, -1, k)
        right = [(j, (j + 1) % n) for j in range(n)]
        left = [(j, (j - 1) % n) for j in range(n)]
        half = k // 2
        pieces = [(0, x, 0, k)]
        r = l = x
        for d in range(1, n // 2 + 1):
            if d < n - d:
                r = lax.ppermute(r, name, right)
                l = lax.ppermute(l, name, left)
                pieces += [(n - d, r, 0, k), (d, l, 0, k)]
            else:
                pieces.append((d, lax.ppermute(r[:, :, :half], name, right), 0, half))
                pieces.append((d, lax.ppermute(l[:, :, half:], name, left), half, k))
        out = None
        for m, v, lo, hi in pieces:
            part = jnp.einsum("tjk,wjkn->wtn", toks[m][:, :, lo:hi], v, preferred_element_type=jnp.float32)
            out = part if out is None else out + part
        return out

    out_a = last_stage(a, "z", tok_a)
    out_b = last_stage(b, "y", tok_b)
    return jnp.concatenate([out_a, out_b], axis=-1)


def local(tokens, w_query, w_key, w_value):
    tok_rows = tokens.shape[0]
    width_group = w_query.shape[1]
    head_count = width_group // DH
    split = width_group // 2
    qkv = project(tokens, [w_query, w_key, w_value], split).astype(jnp.bfloat16)
    qkv = qkv.reshape(3, tok_rows, head_count, DH)
    query_rows, key_rows, value_rows = qkv[0], qkv[1], qkv[2]
    own_total = jnp.einsum("khd,khe->hde", key_rows, value_rows, preferred_element_type=jnp.float32)
    start_state = prefix_over_ctx(own_total)
    causal_mask = jnp.tril(jnp.ones((BLOCK, BLOCK), dtype=bool))
    scores = jnp.einsum("qhd,khd->hqk", query_rows, key_rows, preferred_element_type=jnp.float32)
    scores = jnp.where(causal_mask[None], scores, 0.0).astype(jnp.bfloat16)
    local_term = jnp.einsum("hqk,khd->qhd", scores, value_rows, preferred_element_type=jnp.float32)
    carried = jnp.einsum(
        "qhd,hde->qhe",
        query_rows.astype(jnp.float32),
        start_state,
        precision=lax.Precision.HIGHEST,
    )
    attended_raw = carried + local_term
    scale_inv = lax.rsqrt(jnp.mean(attended_raw * attended_raw, axis=-1, keepdims=True) + epsilon)
    return (attended_raw * scale_inv).astype(jnp.bfloat16).reshape(tok_rows, width_group)


def solution(mesh):
    fine = fine_mesh(mesh)
    return jax.shard_map(
        local,
        mesh=fine,
        in_specs=(P(CTX, None), P(CTX, "hd"), P(CTX, "hd"), P(CTX, "hd")),
        out_specs=P(CTX, "hd"),
        check_vma=False,
    )
```

```python
import jax
import jax.numpy as jnp
from jax import lax
from jax.sharding import Mesh
from jax.sharding import PartitionSpec as P

DH = 128
BLOCK = 512
epsilon = 1e-06

FINE = (("z", 8), ("xh", 2), ("y", 4))
CTX = tuple(name for name, _ in FINE)
SIZES = dict(FINE)


def fine_mesh(mesh):
    devices = mesh.devices.reshape(*SIZES.values(), mesh.devices.shape[1])
    return Mesh(devices, (*CTX, "hd"))


def ring_values(x, name, n):
    right = [(j, (j + 1) % n) for j in range(n)]
    left = [(j, (j - 1) % n) for j in range(n)]
    got = []
    r = l = x
    for k in range(1, n // 2 + 1):
        r = lax.ppermute(r, name, right)
        got.append((k, r))
        if k < n - k:
            l = lax.ppermute(l, name, left)
            got.append((n - k, l))
    return got


def ring_gather(x, name, axis):
    n = SIZES[name]
    by_ahead = {0: x}
    for k, v in ring_values(x, name, n):
        by_ahead[(n - k) % n] = v
    stacked = jnp.stack([by_ahead[m] for m in range(n)], axis=axis)
    return jnp.roll(stacked, lax.axis_index(name), axis=axis)


def direct_values(x, name, n):
    size = SIZES[name]
    got = []
    for k in range(1, n):
        pairs = [(j, j - j % n + (j % n + k) % n) for j in range(size)]
        got.append((k, lax.ppermute(x, name, pairs)))
    return got


def exclusive_and_total(x, name, n=None):
    n = n or SIZES[name]
    idx = lax.axis_index(name) % n
    before = jnp.zeros_like(x)
    total = x
    for k, v in direct_values(x, name, n):
        before = before + jnp.where(k <= idx, v, 0.0)
        total = total + v
    return before, total


def prefix_over_ctx(state):
    before_y, total_y = exclusive_and_total(state, "y")
    before_x, total_xy = exclusive_and_total(total_y, "xh")
    zi = lax.axis_index("z")
    before_z = jnp.zeros_like(state)
    total = total_xy
    bit = 1
    while bit < SIZES["z"]:
        other = lax.ppermute(total, "z", [(j, j ^ bit) for j in range(SIZES["z"])])
        before_z = before_z + jnp.where((zi & bit) != 0, other, 0.0)
        total = total + other
        bit *= 2
    return before_z + before_x + before_y


def project(tokens, ws, split):
    w = jnp.stack(ws)
    other = lax.ppermute(w, "xh", [(0, 1), (1, 0)])
    g = jnp.roll(jnp.stack([w, other], axis=1), lax.axis_index("xh"), axis=1)
    a, b = g[..., :split], g[..., split:]
    a = ring_gather(a, "y", axis=1)
    b = ring_gather(b, "z", axis=1)
    t = tokens.shape[0]
    k = w.shape[1]
    tok = tokens.reshape(t, SIZES["z"], SIZES["xh"], SIZES["y"], k)
    tok_a = jnp.roll(tok.transpose(1, 0, 3, 2, 4), -lax.axis_index("z"), axis=0).reshape(SIZES["z"], t, -1)
    tok_b = jnp.roll(tok.transpose(3, 0, 1, 2, 4), -lax.axis_index("y"), axis=0).reshape(SIZES["y"], t, -1)

    def last_stage(x, name, toks):
        n = SIZES[name]
        count = len(ws)
        x = x.reshape(count, -1, k, x.shape[-1])
        toks = toks.reshape(n, t, -1, k)
        right = [(j, (j + 1) % n) for j in range(n)]
        left = [(j, (j - 1) % n) for j in range(n)]
        half = k // 2
        pieces = [(0, x, 0, k)]
        r = l = x
        for d in range(1, n // 2 + 1):
            if d < n - d:
                r = lax.ppermute(r, name, right)
                l = lax.ppermute(l, name, left)
                pieces += [(n - d, r, 0, k), (d, l, 0, k)]
            else:
                pieces.append((d, lax.ppermute(r[:, :, :half], name, right), 0, half))
                pieces.append((d, lax.ppermute(l[:, :, half:], name, left), half, k))
        out = None
        for m, v, lo, hi in pieces:
            part = jnp.einsum("tjk,wjkn->wtn", toks[m][:, :, lo:hi], v, preferred_element_type=jnp.float32)
            out = part if out is None else out + part
        return out

    out_a = last_stage(a, "z", tok_a)
    out_b = last_stage(b, "y", tok_b)
    return jnp.concatenate([out_a, out_b], axis=-1)


def local(tokens, w_query, w_key, w_value):
    tok_rows = tokens.shape[0]
    width_group = w_query.shape[1]
    head_count = width_group // DH
    split = width_group // 2
    qkv = project(tokens, [w_query, w_key, w_value], split).astype(jnp.bfloat16)
    qkv = qkv.reshape(3, tok_rows, head_count, DH)
    query_rows, key_rows, value_rows = qkv[0], qkv[1], qkv[2]
    own_total = jnp.einsum("khd,khe->hde", key_rows, value_rows, preferred_element_type=jnp.float32)
    start_state = prefix_over_ctx(own_total)
    causal_mask = jnp.tril(jnp.ones((BLOCK, BLOCK), dtype=bool))
    scores = jnp.einsum("qhd,khd->hqk", query_rows, key_rows, preferred_element_type=jnp.float32)
    scores = jnp.where(causal_mask[None], scores, 0.0).astype(jnp.bfloat16)
    local_term = jnp.einsum("hqk,khd->qhd", scores, value_rows, preferred_element_type=jnp.float32)
    carried = jnp.einsum(
        "qhd,hde->qhe",
        query_rows.astype(jnp.float32),
        start_state,
        precision=lax.Precision.HIGHEST,
    )
    attended_raw = carried + local_term
    scale_inv = lax.rsqrt(jnp.mean(attended_raw * attended_raw, axis=-1, keepdims=True) + epsilon)
    return (attended_raw * scale_inv).astype(jnp.bfloat16).reshape(tok_rows, width_group)


def solution(mesh):
    fine = fine_mesh(mesh)
    return jax.shard_map(
        local,
        mesh=fine,
        in_specs=(P(CTX, None), P(CTX, "hd"), P(CTX, "hd"), P(CTX, "hd")),
        out_specs=P(CTX, "hd"),
        check_vma=False,
    )
```
